512 devices in a mesh: fsdp: 32 (over x_lo, z), tp: 16 (over x_hi, y, core).
Axes of the slice: x: 4 (x_hi: 2, x_lo: 2; x = x_hi * 2 + x_lo), y: 4, z: 16, core: 2. Of those that a mesh axis runs over, the one named last changes fastest.
Arguments:
- activations: bfloat16 [16384, 4096], P(('fsdp', 'tp')), may hold values from -6 to 6
- norm_gain: float32 [4096], replicated, may hold values from 0.5 to 1.5
- proj_weight: bfloat16 [3, 4096, 4096], P(None, 'fsdp', 'tp'), may hold values from -0.09375 to 0.09375
- short_filter: float32 [256, 7], P('tp'), may hold values from -3 to 3
- segment_ids: int32 [32, 512], P('fsdp'), may hold values from 0 to 7, never falling along the last dimension, each value on 1 to 256 neighbouring positions
- needle_pos: int32 [32, 16], P('fsdp'), may hold values from 0 to 511
- readout: float32 [4096], replicated, may hold values from -6 to 6
Outputs:
- mixer_out: bfloat16 [16384, 4096], P(('fsdp', 'tp'))
- needle_score: float32 [32, 16], P('fsdp')
The draws below stay inside these ranges and needn't reach their ends.
Inputs may be any that keep to these rules, and one draw needn't show every extreme that they name: segment_ids never fall along a slab; each document covers 1 to 256 positions.
All inputs are finite; a program needn't handle non-finite values.
Results may differ from the reference program's by a relative error of at most 0.0068.
Values may be sent and summed in bfloat16 or wider, within the bound.
No kernel may reach another device: no remote copies, remote signals or barrier semaphores. Data moves between devices by JAX's collectives and lax.ppermute only.
A program may use at most 64 MiB of HBM per device.

```python
import math
import jax
import jax.numpy as jnp
import numpy as np
from jax import lax

D = 4096
GROUP = 16
TAPS = 7
DOCS = 8
NEEDLES = 16
FGROUPS = 256
SLAB = 512
SLABS = 32
TOKENS = 16384


def set_ends(entries, own_key, least, top_value):
    longest = entries.shape.index(max(entries.shape))
    spots = []
    for shift in (0, 1):
        where = [jax.random.randint(jax.random.fold_in(own_key, axis), (), 0, length) for axis, length in enumerate(entries.shape)]
        where[longest] = (where[longest] + shift) % entries.shape[longest]
        spots.append(tuple(where))
    return entries.at[spots[0]].set(least).at[spots[1]].set(top_value)


def level_of(key, shape, shards, low, high):
    def one(position, parts):
        heights = jax.random.uniform(jax.random.fold_in(jax.random.fold_in(key, 6), position), (parts,), jnp.float32, low / len(shards), high / len(shards))
        return jnp.repeat(jnp.exp(heights), shape[position] // parts).reshape((-1,) + (1,) * (len(shape) - position - 1))

    loudness = one(*shards[0])
    for cut in shards[1:]:
        loudness = loudness * one(*cut)
    return loudness


def split_up(amount, total, bound, skew):
    portions = [(1 << 20) // math.isqrt(rank ** skew) + 1 for rank in range(2, amount + 1)]
    spare, given = total - bound - (amount - 1), [1] * (amount - 1)
    while spare > 0:
        free = [i for i in range(amount - 1) if given[i] < bound]
        mass, left = sum([portions[i] for i in free]), spare
        for i in free:
            addition = min(bound - given[i], max(1, left * portions[i] // mass), spare)
            given[i] = given[i] + addition
            spare = spare - addition
    return np.array([bound] + given)


def uneven(rng, amount, total, most, lean):
    if amount == 2:
        one = jax.random.randint(rng, (), max(1, total - most), min(most, total - 1) + 1)
        return jnp.stack([one, total - one])
    tallies = jnp.asarray(split_up(amount, total, most, lean), jnp.int32)
    pairs = (amount - 1) // 2
    donor, sink = tallies[1:1 + 2 * pairs:2], tallies[2:2 + 2 * pairs:2]
    slack = jnp.minimum(donor - 1, most - sink)
    moved = jax.random.randint(jax.random.fold_in(rng, 1), (pairs,), 0, 1 << 20) % (slack + 1)
    tallies = tallies.at[1:1 + 2 * pairs:2].set(donor - moved).at[2:2 + 2 * pairs:2].set(sink + moved)
    return tallies[jax.random.permutation(jax.random.fold_in(rng, 2), amount)]


def centred(key, shape, spread, limit, split=(), held_as=jnp.bfloat16):
    drawn = spread * jax.random.normal(key, shape, jnp.float32)
    if split:
        drawn = drawn * level_of(key, shape, split, -0.22, 0.18)
    return jnp.clip(drawn, -limit, limit).astype(held_as)


def setup_inputs(seed: int = 0) -> dict:
    seeds = jax.random.split(jax.random.key(seed), 8)
    return {
        "activations": centred(seeds[0], (TOKENS, D), 1.0, 6.0, ((0, 512),)),
        "norm_gain": jnp.clip(1.0 + 0.1 * jax.random.normal(seeds[1], (D,), jnp.float32), 0.5, 1.5),
        "proj_weight": centred(seeds[2], (3, D, D), D ** -0.5, 0.09375, ((1, 32), (2, 16))),
        "short_filter": centred(seeds[3], (FGROUPS, TAPS), 0.5, 3.0, ((0, 16),), jnp.float32),
        "segment_ids": jax.vmap(lambda own: jnp.searchsorted(jnp.cumsum(uneven(own, DOCS, SLAB, SLAB // 2, 0)), jnp.arange(SLAB), side="right"))(jax.random.split(seeds[4], SLABS)).reshape((SLABS, SLAB)).astype(jnp.int32),
        "needle_pos": set_ends(jax.random.randint(seeds[5], (SLABS, NEEDLES), 0, SLAB), jax.random.fold_in(seeds[5], 1), 0, SLAB - 1).astype(jnp.int32),
        "readout": centred(seeds[6], (D,), 1.0, 6.0, (), jnp.float32),
    }


EPSILON = 1e-06

def short_conv(gated_prod, tap_table, segments):
    length = gated_prod.shape[0]
    filtered = jnp.zeros(gated_prod.shape, jnp.float32)
    for offset in range(tap_table.shape[1]):
        shifted = jnp.pad(gated_prod, ((offset, 0), (0, 0)))[:length]
        earlier = jnp.pad(segments, (offset, 0), constant_values=-1)[:length]
        same_doc = (earlier == segments).astype(jnp.float32)
        filtered = filtered + shifted * same_doc[:, None] * tap_table[:, offset][None, :]
    return filtered

def reference(activations, norm_gain, proj_weight, short_filter, segment_ids, needle_pos, readout):
    values = activations.astype(jnp.float32)
    scaled = lax.rsqrt(lax.optimization_barrier(jnp.mean(values * values, axis=1, keepdims=True)) + EPSILON)
    normed = (values * scaled * norm_gain[None, :]).astype(jnp.bfloat16)
    slabs_in = normed.reshape(SLABS, SLAB, D)
    tap_table = jnp.repeat(short_filter, GROUP, axis=0)

    def one_slab(inputs):
        slab_in, segments = inputs
        query_part = jnp.dot(slab_in, proj_weight[0], preferred_element_type=jnp.float32)
        key_part = jnp.dot(slab_in, proj_weight[1], preferred_element_type=jnp.float32)
        value_part = jnp.dot(slab_in, proj_weight[2], preferred_element_type=jnp.float32)
        filtered = short_conv(key_part * value_part, tap_table, segments)
        return (query_part * filtered).astype(jnp.bfloat16)
    mixed_slabs = lax.map(one_slab, (slabs_in, segment_ids))
    picked = jnp.take_along_axis(mixed_slabs, needle_pos[:, :, None], axis=1).astype(jnp.float32)
    needle_score = lax.optimization_barrier(jnp.sum(picked * readout[None, None, :], axis=2)) / math.sqrt(D)
    return (mixed_slabs.reshape(TOKENS, D), needle_score)
```

```python
import math

import jax
import jax.numpy as jnp
from jax import lax
from jax.sharding import PartitionSpec as P

EPSILON = 1e-06


def short_conv(gated_prod, tap_table, segments):
    length = gated_prod.shape[0]
    filtered = jnp.zeros(gated_prod.shape, jnp.float32)
    for offset in range(tap_table.shape[1]):
        shifted = jnp.pad(gated_prod, ((offset, 0), (0, 0)))[:length]
        earlier = jnp.pad(segments, (offset, 0), constant_values=-1)[:length]
        same_doc = (earlier == segments).astype(jnp.float32)
        filtered = filtered + shifted * same_doc[:, None] * tap_table[:, offset][None, :]
    return filtered


def local(activations, norm_gain, proj_weight, short_filter, segment_ids, needle_pos, readout):
    model_width = activations.shape[1]
    local_rows = activations.shape[0]
    tp_size = lax.axis_size("tp")
    channels = proj_weight.shape[2]
    weights = lax.all_gather(proj_weight, "fsdp", axis=1, tiled=True)
    values = activations.astype(jnp.float32)
    scaled = lax.rsqrt(jnp.mean(values * values, axis=1, keepdims=True) + EPSILON)
    normed = (values * scaled * norm_gain[None, :]).astype(jnp.bfloat16)
    spread = jnp.broadcast_to(normed[None], (tp_size,) + normed.shape)
    slab_rows = lax.all_to_all(spread, "tp", 0, 0, tiled=False).reshape(
        tp_size * local_rows, model_width
    )
    projected = jnp.einsum("sk,ikc->isc", slab_rows, weights, preferred_element_type=jnp.float32)
    gated_prod = projected[1] * projected[2]
    tap_table = jnp.repeat(short_filter, channels // short_filter.shape[0], axis=0)
    filtered = short_conv(gated_prod, tap_table, segment_ids[0])
    mixed_local = (projected[0] * filtered).astype(jnp.bfloat16)
    device_rank = lax.axis_index("tp")
    positions = needle_pos[0]
    slab_len = tp_size * local_rows
    picker = (positions[:, None] == jnp.arange(slab_len, dtype=jnp.int32)[None, :]).astype(
        jnp.bfloat16
    )
    picked = jnp.dot(picker, mixed_local, preferred_element_type=jnp.float32)
    own_readout = lax.dynamic_slice_in_dim(readout, device_rank * channels, channels, 0)
    partial_sum = jnp.sum(picked * own_readout[None, :], axis=1)
    partials = lax.all_to_all(
        jnp.broadcast_to(partial_sum[None], (tp_size,) + partial_sum.shape), "tp", 0, 0, tiled=False
    )
    needle_score = (jnp.sum(partials, axis=0) / math.sqrt(model_width))[None, :]
    blocks = mixed_local.reshape(tp_size, local_rows, channels)
    gathered = lax.all_to_all(blocks, "tp", 0, 0, tiled=False)
    own_rows = jnp.transpose(gathered, (1, 0, 2)).reshape(local_rows, tp_size * channels)
    return (own_rows, needle_score)


def solution(mesh):
    in_specs = (
        P(("fsdp", "tp"), None),
        P(),
        P(None, "fsdp", "tp"),
        P("tp", None),
        P("fsdp", None),
        P("fsdp", None),
        P(),
    )
    out_specs = (P(("fsdp", "tp"), None), P("fsdp", None))
    return jax.shard_map(local, mesh=mesh, in_specs=in_specs, out_specs=out_specs, check_vma=False)
```

```python
import math

import jax
import jax.numpy as jnp
from jax import lax
from jax.sharding import PartitionSpec as P

EPSILON = 1e-06


def short_conv(gated_prod, tap_table, segments):
    length = gated_prod.shape[0]
    filtered = jnp.zeros(gated_prod.shape, jnp.float32)
    for offset in range(tap_table.shape[1]):
        shifted = jnp.pad(gated_prod, ((offset, 0), (0, 0)))[:length]
        earlier = jnp.pad(segments, (offset, 0), constant_values=-1)[:length]
        same_doc = (earlier == segments).astype(jnp.float32)
        filtered = filtered + shifted * same_doc[:, None] * tap_table[:, offset][None, :]
    return filtered


def gather_weights(proj_weight, fsdp_size, z_size):
    fsdp = lax.axis_index("fsdp")
    x_lo = fsdp // z_size
    x_swap = [(f, (f + z_size) % fsdp_size) for f in range(fsdp_size)]
    z_up = [(f, (f // z_size) * z_size + (f + 1) % z_size) for f in range(fsdp_size)]
    z_down = [(f, (f // z_size) * z_size + (f - 1) % z_size) for f in range(fsdp_size)]
    other = lax.ppermute(proj_weight, "fsdp", x_swap)
    first = jnp.where(x_lo == 0, proj_weight, other)
    second = jnp.where(x_lo == 0, other, proj_weight)
    pair = jnp.stack([first, second], axis=1)
    ahead = [pair]
    behind = []
    right = pair
    left = pair
    for _ in range(1, z_size // 2):
        right = lax.ppermute(right, "fsdp", z_up)
        left = lax.ppermute(left, "fsdp", z_down)
        behind.append(right)
        ahead.append(left)
    last_a = lax.ppermute(right[:, :1], "fsdp", z_up)
    last_b = lax.ppermute(left[:, 1:], "fsdp", z_down)
    ahead.append(jnp.concatenate([last_a, last_b], axis=1))
    pieces = ahead + behind[::-1]
    stacked = jnp.stack(pieces, axis=2)
    return stacked.reshape(
        proj_weight.shape[0], fsdp_size * proj_weight.shape[1], proj_weight.shape[2]
    )


def local(activations, norm_gain, proj_weight, short_filter, segment_ids, needle_pos, readout):
    model_width = activations.shape[1]
    local_rows = activations.shape[0]
    tp_size = lax.axis_size("tp")
    fsdp_size = lax.axis_size("fsdp")
    z_size = fsdp_size // 2
    channels = proj_weight.shape[2]
    block = proj_weight.shape[1]
    weights = gather_weights(proj_weight, fsdp_size, z_size)
    values = activations.astype(jnp.float32)
    scaled = lax.rsqrt(jnp.mean(values * values, axis=1, keepdims=True) + EPSILON)
    normed = (values * scaled * norm_gain[None, :]).astype(jnp.bfloat16)
    z = lax.axis_index("fsdp") % z_size
    grid = normed.reshape(local_rows, 2, z_size, block)
    doubled = jnp.concatenate([grid, grid], axis=2)
    rotated = lax.dynamic_slice_in_dim(doubled, z, z_size, axis=2).reshape(local_rows, model_width)
    spread = jnp.broadcast_to(rotated[None], (tp_size,) + rotated.shape)
    slab_rows = lax.all_to_all(spread, "tp", 0, 0, tiled=False).reshape(
        tp_size * local_rows, model_width
    )
    projected = jnp.einsum("sk,ikc->isc", slab_rows, weights, preferred_element_type=jnp.float32)
    gated_prod = projected[1] * projected[2]
    tap_table = jnp.repeat(short_filter, channels // short_filter.shape[0], axis=0)
    filtered = short_conv(gated_prod, tap_table, segment_ids[0])
    mixed_local = (projected[0] * filtered).astype(jnp.bfloat16)
    device_rank = lax.axis_index("tp")
    positions = needle_pos[0]
    slab_len = tp_size * local_rows
    picker = (positions[:, None] == jnp.arange(slab_len, dtype=jnp.int32)[None, :]).astype(
        jnp.bfloat16
    )
    picked = jnp.dot(picker, mixed_local, preferred_element_type=jnp.float32)
    own_readout = lax.dynamic_slice_in_dim(readout, device_rank * channels, channels, 0)
    partial_sum = jnp.sum(picked * own_readout[None, :], axis=1)
    partials = lax.all_to_all(
        jnp.broadcast_to(partial_sum[None], (tp_size,) + partial_sum.shape), "tp", 0, 0, tiled=False
    )
    needle_score = (jnp.sum(partials, axis=0) / math.sqrt(model_width))[None, :]
    blocks = mixed_local.reshape(tp_size, local_rows, channels)
    gathered = lax.all_to_all(blocks, "tp", 0, 0, tiled=False)
    own_rows = jnp.transpose(gathered, (1, 0, 2)).reshape(local_rows, tp_size * channels)
    return (own_rows, needle_score)


def solution(mesh):
    in_specs = (
        P(("fsdp", "tp"), None),
        P(),
        P(None, "fsdp", "tp"),
        P("tp", None),
        P("fsdp", None),
        P("fsdp", None),
        P(),
    )
    out_specs = (P(("fsdp", "tp"), None), P("fsdp", None))
    return jax.shard_map(local, mesh=mesh, in_specs=in_specs, out_specs=out_specs, check_vma=False)
```

```python
import math

import jax
import jax.numpy as jnp
from jax import lax
from jax.experimental.layout import Layout, with_layout_constraint
from jax.sharding import PartitionSpec as P

EPSILON = 1e-06


def short_conv(gated_prod, tap_table, segments):
    length = gated_prod.shape[0]
    filtered = jnp.zeros(gated_prod.shape, jnp.float32)
    for offset in range(tap_table.shape[1]):
        shifted = jnp.pad(gated_prod, ((offset, 0), (0, 0)))[:length]
        earlier = jnp.pad(segments, (offset, 0), constant_values=-1)[:length]
        same_doc = (earlier == segments).astype(jnp.float32)
        filtered = filtered + shifted * same_doc[:, None] * tap_table[:, offset][None, :]
    return filtered


def gather_weights(proj_weight, fsdp_size, z_size):
    fsdp = lax.axis_index("fsdp")
    x_lo = fsdp // z_size
    x_swap = [(f, (f + z_size) % fsdp_size) for f in range(fsdp_size)]
    z_up = [(f, (f // z_size) * z_size + (f + 1) % z_size) for f in range(fsdp_size)]
    z_down = [(f, (f // z_size) * z_size + (f - 1) % z_size) for f in range(fsdp_size)]
    other = lax.ppermute(proj_weight, "fsdp", x_swap)
    first = jnp.where(x_lo == 0, proj_weight, other)
    second = jnp.where(x_lo == 0, other, proj_weight)
    pair = jnp.stack([first, second], axis=1)
    ahead = [pair]
    behind = []
    right = pair
    left = pair
    for _ in range(1, z_size // 2):
        right = lax.ppermute(right, "fsdp", z_up)
        left = lax.ppermute(left, "fsdp", z_down)
        behind.append(right)
        ahead.append(left)
    last_a = lax.ppermute(right[:, :1], "fsdp", z_up)
    last_b = lax.ppermute(left[:, 1:], "fsdp", z_down)
    ahead.append(jnp.concatenate([last_a, last_b], axis=1))
    pieces = ahead + behind[::-1]
    stacked = with_layout_constraint(jnp.stack(pieces, axis=2), Layout((0, 1, 2, 3, 4)))
    return stacked.reshape(
        proj_weight.shape[0], fsdp_size * proj_weight.shape[1], proj_weight.shape[2]
    )


def local(activations, norm_gain, proj_weight, short_filter, segment_ids, needle_pos, readout):
    model_width = activations.shape[1]
    local_rows = activations.shape[0]
    tp_size = lax.axis_size("tp")
    fsdp_size = lax.axis_size("fsdp")
    z_size = fsdp_size // 2
    channels = proj_weight.shape[2]
    block = proj_weight.shape[1]
    weights = gather_weights(proj_weight, fsdp_size, z_size)
    values = activations.astype(jnp.float32)
    scaled = lax.rsqrt(jnp.mean(values * values, axis=1, keepdims=True) + EPSILON)
    normed = (values * scaled * norm_gain[None, :]).astype(jnp.bfloat16)
    z = lax.axis_index("fsdp") % z_size
    grid = normed.reshape(local_rows, 2, z_size, block)
    doubled = jnp.concatenate([grid, grid], axis=2)
    rotated = lax.dynamic_slice_in_dim(doubled, z, z_size, axis=2).reshape(local_rows, model_width)
    spread = jnp.broadcast_to(rotated[None], (tp_size,) + rotated.shape)
    slab_rows = lax.all_to_all(spread, "tp", 0, 0, tiled=False).reshape(
        tp_size * local_rows, model_width
    )
    projected = jnp.einsum("sk,ikc->isc", slab_rows, weights, preferred_element_type=jnp.float32)
    projected = with_layout_constraint(projected, Layout((0, 1, 2)))
    gated_prod = projected[1] * projected[2]
    tap_table = jnp.repeat(short_filter, channels // short_filter.shape[0], axis=0)
    filtered = short_conv(gated_prod, tap_table, segment_ids[0])
    mixed_local = (projected[0] * filtered).astype(jnp.bfloat16)
    device_rank = lax.axis_index("tp")
    positions = needle_pos[0]
    slab_len = tp_size * local_rows
    picker = (positions[:, None] == jnp.arange(slab_len, dtype=jnp.int32)[None, :]).astype(
        jnp.bfloat16
    )
    picked = jnp.dot(picker, mixed_local, preferred_element_type=jnp.float32)
    own_readout = lax.dynamic_slice_in_dim(readout, device_rank * channels, channels, 0)
    partial_sum = jnp.sum(picked * own_readout[None, :], axis=1)
    high = partial_sum.astype(jnp.bfloat16)
    low = (partial_sum - high.astype(jnp.float32)).astype(jnp.bfloat16)
    extra_rows = 16
    extra = jnp.zeros((extra_rows, channels), jnp.bfloat16)
    extra = extra.at[0, : high.shape[0]].set(high).at[1, : low.shape[0]].set(low)
    blocks = mixed_local.reshape(tp_size, local_rows, channels)
    payload = jnp.concatenate(
        [blocks, jnp.broadcast_to(extra[None], (tp_size, extra_rows, channels))], axis=1
    )
    gathered = lax.all_to_all(payload, "tp", 0, 0, tiled=False)
    own_rows = jnp.transpose(gathered[:, :local_rows], (1, 0, 2)).reshape(
        local_rows, tp_size * channels
    )
    count = positions.shape[0]
    received = gathered[:, local_rows, :count].astype(jnp.float32) + gathered[
        :, local_rows + 1, :count
    ].astype(jnp.float32)
    needle_score = (jnp.sum(received, axis=0) / math.sqrt(model_width))[None, :]
    return (own_rows, needle_score)


def solution(mesh):
    in_specs = (
        P(("fsdp", "tp"), None),
        P(),
        P(None, "fsdp", "tp"),
        P("tp", None),
        P("fsdp", None),
        P("fsdp", None),
        P(),
    )
    out_specs = (P(("fsdp", "tp"), None), P("fsdp", None))
    return jax.shard_map(local, mesh=mesh, in_specs=in_specs, out_specs=out_specs, check_vma=False)
```

```python
import math

import jax
import jax.numpy as jnp
from jax import lax
from jax.experimental.layout import Layout, with_layout_constraint
from jax.sharding import PartitionSpec as P

EPSILON = 1e-06


def short_conv(gated_prod, tap_table, segments):
    length = gated_prod.shape[0]
    filtered = jnp.zeros(gated_prod.shape, jnp.float32)
    for offset in range(tap_table.shape[1]):
        shifted = jnp.pad(gated_prod, ((offset, 0), (0, 0)))[:length]
        earlier = jnp.pad(segments, (offset, 0), constant_values=-1)[:length]
        same_doc = (earlier == segments).astype(jnp.float32)
        filtered = filtered + shifted * same_doc[:, None] * tap_table[:, offset][None, :]
    return filtered


def ring_gather(part, fsdp_size, z_size):
    fsdp = lax.axis_index("fsdp")
    x_lo = fsdp // z_size
    z = fsdp % z_size
    x_swap = [(f, (f + z_size) % fsdp_size) for f in range(fsdp_size)]
    z_up = [(f, (f // z_size) * z_size + (f + 1) % z_size) for f in range(fsdp_size)]
    z_down = [(f, (f // z_size) * z_size + (f - 1) % z_size) for f in range(fsdp_size)]
    other = lax.ppermute(part, "fsdp", x_swap)
    first = jnp.where(x_lo == 0, part, other)
    second = jnp.where(x_lo == 0, other, part)
    pair = jnp.stack([first, second], axis=1)
    lead, halves, block, width = pair.shape
    buffer = with_layout_constraint(
        jnp.zeros((lead, halves, z_size, block, width), part.dtype), Layout((0, 1, 2, 3, 4))
    )

    def put(into, piece, at):
        return lax.dynamic_update_slice(into, piece[:, :, None], (0, 0, at, 0, 0))

    buffer = put(buffer, pair, z)
    right = pair
    left = pair
    for step in range(1, z_size // 2):
        right = lax.ppermute(right, "fsdp", z_up)
        left = lax.ppermute(left, "fsdp", z_down)
        buffer = put(buffer, right, (z - step) % z_size)
        buffer = put(buffer, left, (z + step) % z_size)
    last_a = lax.ppermute(right[:, :1], "fsdp", z_up)
    last_b = lax.ppermute(left[:, 1:], "fsdp", z_down)
    buffer = put(buffer, jnp.concatenate([last_a, last_b], axis=1), (z + z_size // 2) % z_size)
    buffer = with_layout_constraint(buffer, Layout((0, 1, 2, 3, 4)))
    return buffer.reshape(lead, fsdp_size * block, width)


def local(activations, norm_gain, proj_weight, short_filter, segment_ids, needle_pos, readout):
    model_width = activations.shape[1]
    local_rows = activations.shape[0]
    tp_size = lax.axis_size("tp")
    fsdp_size = lax.axis_size("fsdp")
    z_size = fsdp_size // 2
    channels = proj_weight.shape[2]
    query_weights = lax.all_gather(proj_weight[0], "fsdp", axis=0, tiled=True)
    pair_weights = ring_gather(proj_weight[1:], fsdp_size, z_size)
    values = activations.astype(jnp.float32)
    scaled = lax.rsqrt(jnp.mean(values * values, axis=1, keepdims=True) + EPSILON)
    normed = (values * scaled * norm_gain[None, :]).astype(jnp.bfloat16)
    spread = jnp.broadcast_to(normed[None], (tp_size,) + normed.shape)
    slab_rows = lax.all_to_all(spread, "tp", 0, 0, tiled=False).reshape(
        tp_size * local_rows, model_width
    )
    key_value = jnp.einsum(
        "sk,ikc->isc", slab_rows, pair_weights, preferred_element_type=jnp.float32
    )
    key_value = with_layout_constraint(key_value, Layout((0, 1, 2)))
    query_part = jnp.dot(slab_rows, query_weights, preferred_element_type=jnp.float32)
    projected = (query_part, key_value[0], key_value[1])
    gated_prod = projected[1] * projected[2]
    tap_table = jnp.repeat(short_filter, channels // short_filter.shape[0], axis=0)
    filtered = short_conv(gated_prod, tap_table, segment_ids[0])
    mixed_local = (projected[0] * filtered).astype(jnp.bfloat16)
    device_rank = lax.axis_index("tp")
    positions = needle_pos[0]
    slab_len = tp_size * local_rows
    picker = (positions[:, None] == jnp.arange(slab_len, dtype=jnp.int32)[None, :]).astype(
        jnp.bfloat16
    )
    picked = jnp.dot(picker, mixed_local, preferred_element_type=jnp.float32)
    own_readout = lax.dynamic_slice_in_dim(readout, device_rank * channels, channels, 0)
    partial_sum = jnp.sum(picked * own_readout[None, :], axis=1)
    rounded = lax.reduce_precision(partial_sum, exponent_bits=8, mantissa_bits=7)
    high = rounded.astype(jnp.bfloat16)
    low = (partial_sum - rounded).astype(jnp.bfloat16)
    extra_rows = 16
    extra = jnp.zeros((extra_rows, channels), jnp.bfloat16)
    extra = extra.at[0, : high.shape[0]].set(high).at[1, : low.shape[0]].set(low)
    blocks = mixed_local.reshape(tp_size, local_rows, channels)
    payload = jnp.concatenate(
        [blocks, jnp.broadcast_to(extra[None], (tp_size, extra_rows, channels))], axis=1
    )
    gathered = lax.all_to_all(payload, "tp", 0, 0, tiled=False)
    own_rows = jnp.transpose(gathered[:, :local_rows], (1, 0, 2)).reshape(
        local_rows, tp_size * channels
    )
    count = positions.shape[0]
    received = gathered[:, local_rows, :count].astype(jnp.float32) + gathered[
        :, local_rows + 1, :count
    ].astype(jnp.float32)
    needle_score = (jnp.sum(received, axis=0) / math.sqrt(model_width))[None, :]
    return (own_rows, needle_score)


def solution(mesh):
    in_specs = (
        P(("fsdp", "tp"), None),
        P(),
        P(None, "fsdp", "tp"),
        P("tp", None),
        P("fsdp", None),
        P("fsdp", None),
        P(),
    )
    out_specs = (P(("fsdp", "tp"), None), P("fsdp", None))
    return jax.shard_map(local, mesh=mesh, in_specs=in_specs, out_specs=out_specs, check_vma=False)
```

```python
import math

import jax
import jax.numpy as jnp
from jax import lax
from jax.experimental.layout import Layout, with_layout_constraint
from jax.sharding import PartitionSpec as P

EPSILON = 1e-06


def short_conv(gated_prod, tap_table, segments):
    length = gated_prod.shape[0]
    filtered = jnp.zeros(gated_prod.shape, jnp.float32)
    for offset in range(tap_table.shape[1]):
        shifted = jnp.pad(gated_prod, ((offset, 0), (0, 0)))[:length]
        earlier = jnp.pad(segments, (offset, 0), constant_values=-1)[:length]
        same_doc = (earlier == segments).astype(jnp.float32)
        filtered = filtered + shifted * same_doc[:, None] * tap_table[:, offset][None, :]
    return filtered


def gather_weights(proj_weight, fsdp_size, z_size):
    fsdp = lax.axis_index("fsdp")
    x_lo = fsdp // z_size
    x_swap = [(f, (f + z_size) % fsdp_size) for f in range(fsdp_size)]
    z_up = [(f, (f // z_size) * z_size + (f + 1) % z_size) for f in range(fsdp_size)]
    z_down = [(f, (f // z_size) * z_size + (f - 1) % z_size) for f in range(fsdp_size)]
    other = lax.ppermute(proj_weight, "fsdp", x_swap)
    first = jnp.where(x_lo == 0, proj_weight, other)
    second = jnp.where(x_lo == 0, other, proj_weight)
    pair = jnp.stack([first, second], axis=1)
    ahead = [pair]
    behind = []
    right = pair
    left = pair
    for _ in range(1, z_size // 2):
        right = lax.ppermute(right, "fsdp", z_up)
        left = lax.ppermute(left, "fsdp", z_down)
        behind.append(right)
        ahead.append(left)
    last_a = lax.ppermute(right[:, :1], "fsdp", z_up)
    last_b = lax.ppermute(left[:, 1:], "fsdp", z_down)
    ahead.append(jnp.concatenate([last_a, last_b], axis=1))
    pieces = ahead + behind[::-1]
    stacked = with_layout_constraint(jnp.stack(pieces, axis=2), Layout((0, 1, 2, 3, 4)))
    return stacked.reshape(
        proj_weight.shape[0], fsdp_size * proj_weight.shape[1], proj_weight.shape[2]
    )


def local(activations, norm_gain, proj_weight, short_filter, segment_ids, needle_pos, readout):
    model_width = activations.shape[1]
    local_rows = activations.shape[0]
    tp_size = lax.axis_size("tp")
    fsdp_size = lax.axis_size("fsdp")
    z_size = fsdp_size // 2
    channels = proj_weight.shape[2]
    block = proj_weight.shape[1]
    weights = gather_weights(proj_weight, fsdp_size, z_size)
    values = activations.astype(jnp.float32)
    scaled = lax.rsqrt(jnp.mean(values * values, axis=1, keepdims=True) + EPSILON)
    normed = (values * scaled * norm_gain[None, :]).astype(jnp.bfloat16)
    z = lax.axis_index("fsdp") % z_size
    grid = normed.reshape(local_rows, 2, z_size, block)
    doubled = jnp.concatenate([grid, grid], axis=2)
    rotated = lax.dynamic_slice_in_dim(doubled, z, z_size, axis=2).reshape(local_rows, model_width)
    spread = jnp.broadcast_to(rotated[None], (tp_size,) + rotated.shape)
    slab_rows = lax.all_to_all(spread, "tp", 0, 0, tiled=False).reshape(
        tp_size * local_rows, model_width
    )
    projected = jnp.einsum("sk,ikc->isc", slab_rows, weights, preferred_element_type=jnp.float32)
    projected = with_layout_constraint(projected, Layout((0, 1, 2)))
    gated_prod = projected[1] * projected[2]
    tap_table = jnp.repeat(short_filter, channels // short_filter.shape[0], axis=0)
    filtered = short_conv(gated_prod, tap_table, segment_ids[0])
    mixed_local = (projected[0] * filtered).astype(jnp.bfloat16)
    device_rank = lax.axis_index("tp")
    positions = needle_pos[0]
    slab_len = tp_size * local_rows
    picker = (positions[:, None] == jnp.arange(slab_len, dtype=jnp.int32)[None, :]).astype(
        jnp.bfloat16
    )
    picked = jnp.dot(picker, mixed_local, preferred_element_type=jnp.float32)
    own_readout = lax.dynamic_slice_in_dim(readout, device_rank * channels, channels, 0)
    partial_sum = jnp.sum(picked * own_readout[None, :], axis=1)
    rounded = lax.reduce_precision(partial_sum, exponent_bits=8, mantissa_bits=7)
    high = rounded.astype(jnp.bfloat16)
    low = (partial_sum - rounded).astype(jnp.bfloat16)
    extra_rows = 16
    extra = jnp.zeros((extra_rows, channels), jnp.bfloat16)
    extra = extra.at[0, : high.shape[0]].set(high).at[1, : low.shape[0]].set(low)
    blocks = mixed_local.reshape(tp_size, local_rows, channels)
    payload = jnp.concatenate(
        [blocks, jnp.broadcast_to(extra[None], (tp_size, extra_rows, channels))], axis=1
    )
    gathered = lax.all_to_all(payload, "tp", 0, 0, tiled=False)
    own_rows = jnp.transpose(gathered[:, :local_rows], (1, 0, 2)).reshape(
        local_rows, tp_size * channels
    )
    count = positions.shape[0]
    received = gathered[:, local_rows, :count].astype(jnp.float32) + gathered[
        :, local_rows + 1, :count
    ].astype(jnp.float32)
    needle_score = (jnp.sum(received, axis=0) / math.sqrt(model_width))[None, :]
    return (own_rows, needle_score)


def solution(mesh):
    in_specs = (
        P(("fsdp", "tp"), None),
        P(),
        P(None, "fsdp", "tp"),
        P("tp", None),
        P("fsdp", None),
        P("fsdp", None),
        P(),
    )
    out_specs = (P(("fsdp", "tp"), None), P("fsdp", None))
    return jax.shard_map(local, mesh=mesh, in_specs=in_specs, out_specs=out_specs, check_vma=False)
```

```python
import math

import jax
import jax.numpy as jnp
from jax import lax
from jax.experimental.layout import Layout, with_layout_constraint
from jax.sharding import PartitionSpec as P

EPSILON = 1e-06


def short_conv(gated_prod, tap_table, segments):
    length = gated_prod.shape[0]
    filtered = jnp.zeros(gated_prod.shape, jnp.float32)
    for offset in range(tap_table.shape[1]):
        shifted = jnp.pad(gated_prod, ((offset, 0), (0, 0)))[:length]
        earlier = jnp.pad(segments, (offset, 0), constant_values=-1)[:length]
        same_doc = (earlier == segments).astype(jnp.float32)
        filtered = filtered + shifted * same_doc[:, None] * tap_table[:, offset][None, :]
    return filtered


def gather_weights(proj_weight, fsdp_size, z_size, companion):
    fsdp = lax.axis_index("fsdp")
    x_lo = fsdp // z_size
    x_swap = [(f, (f + z_size) % fsdp_size) for f in range(fsdp_size)]
    z_up = [(f, (f // z_size) * z_size + (f + 1) % z_size) for f in range(fsdp_size)]
    z_down = [(f, (f // z_size) * z_size + (f - 1) % z_size) for f in range(fsdp_size)]
    other = lax.ppermute(proj_weight, "fsdp", x_swap)
    first = jnp.where(x_lo == 0, proj_weight, other)
    second = jnp.where(x_lo == 0, other, proj_weight)
    pair = jnp.stack([first, second], axis=1)
    ahead = [pair]
    behind = []
    right = pair
    left = pair
    for _ in range(1, z_size // 2):
        right = lax.ppermute(right, "fsdp", z_up)
        left = lax.ppermute(left, "fsdp", z_down)
        behind.append(right)
        ahead.append(left)
    sent_a, sent_b, companion = lax.optimization_barrier((right[:, :1], left[:, 1:], companion))
    last_a = lax.ppermute(sent_a, "fsdp", z_up)
    last_b = lax.ppermute(sent_b, "fsdp", z_down)
    last = jnp.concatenate([last_a, last_b], axis=1)
    stacked = with_layout_constraint(
        jnp.stack(ahead + behind[::-1], axis=1), Layout((0, 1, 2, 3, 4))
    )
    lead, count, halves, block, width = stacked.shape
    early = stacked.reshape(lead, count * halves * block, width)
    return early, last.reshape(lead, halves * block, width), companion


def local(activations, norm_gain, proj_weight, short_filter, segment_ids, needle_pos, readout):
    model_width = activations.shape[1]
    local_rows = activations.shape[0]
    tp_size = lax.axis_size("tp")
    fsdp_size = lax.axis_size("fsdp")
    z_size = fsdp_size // 2
    channels = proj_weight.shape[2]
    block = proj_weight.shape[1]
    values = activations.astype(jnp.float32)
    scaled = lax.rsqrt(jnp.mean(values * values, axis=1, keepdims=True) + EPSILON)
    normed = (values * scaled * norm_gain[None, :]).astype(jnp.bfloat16)
    z = lax.axis_index("fsdp") % z_size
    half = z_size // 2
    grid = jnp.transpose(normed.reshape(local_rows, 2, z_size, block), (0, 2, 1, 3))
    doubled = jnp.concatenate([grid, grid], axis=1)
    ordered = jnp.concatenate(
        [
            lax.dynamic_slice_in_dim(doubled, z, half, axis=1),
            lax.dynamic_slice_in_dim(doubled, z + half + 1, half - 1, axis=1),
            lax.dynamic_slice_in_dim(doubled, z + half, 1, axis=1),
        ],
        axis=1,
    ).reshape(local_rows, model_width)
    spread = jnp.broadcast_to(ordered[None], (tp_size,) + ordered.shape)
    slab_rows = lax.all_to_all(spread, "tp", 0, 0, tiled=False).reshape(
        tp_size * local_rows, model_width
    )
    early_weights, last_weights, slab_rows = gather_weights(
        proj_weight, fsdp_size, z_size, slab_rows
    )
    split = early_weights.shape[1]
    projected = jnp.einsum(
        "sk,ikc->isc", slab_rows[:, :split], early_weights, preferred_element_type=jnp.float32
    ) + jnp.einsum(
        "sk,ikc->isc", slab_rows[:, split:], last_weights, preferred_element_type=jnp.float32
    )
    projected = with_layout_constraint(projected, Layout((0, 1, 2)))
    gated_prod = projected[1] * projected[2]
    tap_table = jnp.repeat(short_filter, channels // short_filter.shape[0], axis=0)
    filtered = short_conv(gated_prod, tap_table, segment_ids[0])
    mixed_local = (projected[0] * filtered).astype(jnp.bfloat16)
    device_rank = lax.axis_index("tp")
    positions = needle_pos[0]
    slab_len = tp_size * local_rows
    picker = (positions[:, None] == jnp.arange(slab_len, dtype=jnp.int32)[None, :]).astype(
        jnp.bfloat16
    )
    picked = jnp.dot(picker, mixed_local, preferred_element_type=jnp.float32)
    own_readout = lax.dynamic_slice_in_dim(readout, device_rank * channels, channels, 0)
    partial_sum = jnp.sum(picked * own_readout[None, :], axis=1)
    rounded = lax.reduce_precision(partial_sum, exponent_bits=8, mantissa_bits=7)
    high = rounded.astype(jnp.bfloat16)
    low = (partial_sum - rounded).astype(jnp.bfloat16)
    extra_rows = 16
    extra = jnp.zeros((extra_rows, channels), jnp.bfloat16)
    extra = extra.at[0, : high.shape[0]].set(high).at[1, : low.shape[0]].set(low)
    blocks = mixed_local.reshape(tp_size, local_rows, channels)
    payload = jnp.concatenate(
        [blocks, jnp.broadcast_to(extra[None], (tp_size, extra_rows, channels))], axis=1
    )
    gathered = lax.all_to_all(payload, "tp", 0, 0, tiled=False)
    own_rows = jnp.transpose(gathered[:, :local_rows], (1, 0, 2)).reshape(
        local_rows, tp_size * channels
    )
    count = positions.shape[0]
    received = gathered[:, local_rows, :count].astype(jnp.float32) + gathered[
        :, local_rows + 1, :count
    ].astype(jnp.float32)
    needle_score = (jnp.sum(received, axis=0) / math.sqrt(model_width))[None, :]
    return (own_rows, needle_score)


def solution(mesh):
    in_specs = (
        P(("fsdp", "tp"), None),
        P(),
        P(None, "fsdp", "tp"),
        P("tp", None),
        P("fsdp", None),
        P("fsdp", None),
        P(),
    )
    out_specs = (P(("fsdp", "tp"), None), P("fsdp", None))
    return jax.shard_map(local, mesh=mesh, in_specs=in_specs, out_specs=out_specs, check_vma=False)
```

```python
import math

import jax
import jax.numpy as jnp
from jax import lax
from jax.experimental.layout import Layout, with_layout_constraint
from jax.sharding import Mesh, PartitionSpec as P

EPSILON = 1e-06
TP = ("chip", "core")


def short_conv(gated_prod, tap_table, segments):
    length = gated_prod.shape[0]
    filtered = jnp.zeros(gated_prod.shape, jnp.float32)
    for offset in range(tap_table.shape[1]):
        shifted = jnp.pad(gated_prod, ((offset, 0), (0, 0)))[:length]
        earlier = jnp.pad(segments, (offset, 0), constant_values=-1)[:length]
        same_doc = (earlier == segments).astype(jnp.float32)
        filtered = filtered + shifted * same_doc[:, None] * tap_table[:, offset][None, :]
    return filtered


def gather_weights(proj_weight, fsdp_size, z_size):
    fsdp = lax.axis_index("fsdp")
    x_lo = fsdp // z_size
    x_swap = [(f, (f + z_size) % fsdp_size) for f in range(fsdp_size)]
    z_up = [(f, (f // z_size) * z_size + (f + 1) % z_size) for f in range(fsdp_size)]
    z_down = [(f, (f // z_size) * z_size + (f - 1) % z_size) for f in range(fsdp_size)]
    other = lax.ppermute(proj_weight, "fsdp", x_swap)
    first = jnp.where(x_lo == 0, proj_weight, other)
    second = jnp.where(x_lo == 0, other, proj_weight)
    pair = jnp.stack([first, second], axis=1)
    ahead = [pair]
    behind = []
    right = pair
    left = pair
    for _ in range(1, z_size // 2):
        right = lax.ppermute(right, "fsdp", z_up)
        left = lax.ppermute(left, "fsdp", z_down)
        behind.append(right)
        ahead.append(left)
    last_a = lax.ppermute(right[:, :1], "fsdp", z_up)
    last_b = lax.ppermute(left[:, 1:], "fsdp", z_down)
    ahead.append(jnp.concatenate([last_a, last_b], axis=1))
    pieces = ahead + behind[::-1]
    stacked = with_layout_constraint(jnp.stack(pieces, axis=2), Layout((0, 1, 2, 3, 4)))
    return stacked.reshape(
        proj_weight.shape[0], fsdp_size * proj_weight.shape[1], proj_weight.shape[2]
    )


def local(activations, norm_gain, proj_weight, short_filter, segment_ids, needle_pos, readout):
    model_width = activations.shape[1]
    local_rows = activations.shape[0]
    tp_size = lax.axis_size(TP)
    fsdp_size = lax.axis_size("fsdp")
    z_size = fsdp_size // 2
    channels = proj_weight.shape[2]
    block = proj_weight.shape[1]
    weights = gather_weights(proj_weight, fsdp_size, z_size)
    values = activations.astype(jnp.float32)
    scaled = lax.rsqrt(jnp.mean(values * values, axis=1, keepdims=True) + EPSILON)
    normed = (values * scaled * norm_gain[None, :]).astype(jnp.bfloat16)
    z = lax.axis_index("fsdp") % z_size
    grid = normed.reshape(local_rows, 2, z_size, block)
    doubled = jnp.concatenate([grid, grid], axis=2)
    rotated = lax.dynamic_slice_in_dim(doubled, z, z_size, axis=2).reshape(local_rows, model_width)
    spread = jnp.broadcast_to(rotated[None], (tp_size,) + rotated.shape)
    slab_rows = lax.all_to_all(spread, TP, 0, 0, tiled=False).reshape(
        tp_size * local_rows, model_width
    )
    projected = jnp.einsum("sk,ikc->isc", slab_rows, weights, preferred_element_type=jnp.float32)
    projected = with_layout_constraint(projected, Layout((0, 1, 2)))
    gated_prod = projected[1] * projected[2]
    tap_table = jnp.repeat(short_filter, channels // short_filter.shape[0], axis=0)
    filtered = short_conv(gated_prod, tap_table, segment_ids[0])
    mixed_local = (projected[0] * filtered).astype(jnp.bfloat16)
    device_rank = lax.axis_index(TP)
    positions = needle_pos[0]
    slab_len = tp_size * local_rows
    picker = (positions[:, None] == jnp.arange(slab_len, dtype=jnp.int32)[None, :]).astype(
        jnp.bfloat16
    )
    picked = jnp.dot(picker, mixed_local, preferred_element_type=jnp.float32)
    own_readout = lax.dynamic_slice_in_dim(readout, device_rank * channels, channels, 0)
    partial_sum = jnp.sum(picked * own_readout[None, :], axis=1)
    rounded = lax.reduce_precision(partial_sum, exponent_bits=8, mantissa_bits=7)
    high = rounded.astype(jnp.bfloat16)
    low = (partial_sum - rounded).astype(jnp.bfloat16)
    extra_rows = 16
    extra = jnp.zeros((extra_rows, channels), jnp.bfloat16)
    extra = extra.at[0, : high.shape[0]].set(high).at[1, : low.shape[0]].set(low)
    blocks = mixed_local.reshape(tp_size, local_rows, channels)
    payload = jnp.concatenate(
        [blocks, jnp.broadcast_to(extra[None], (tp_size, extra_rows, channels))], axis=1
    )
    per_chip = payload.reshape((tp_size // 2, 2) + payload.shape[1:])
    paired = lax.all_to_all(per_chip, "core", 1, 1, tiled=False)
    gathered = lax.all_to_all(paired, "chip", 0, 0, tiled=False).reshape(payload.shape)
    own_rows = jnp.transpose(gathered[:, :local_rows], (1, 0, 2)).reshape(
        local_rows, tp_size * channels
    )
    count = positions.shape[0]
    received = gathered[:, local_rows, :count].astype(jnp.float32) + gathered[
        :, local_rows + 1, :count
    ].astype(jnp.float32)
    needle_score = (jnp.sum(received, axis=0) / math.sqrt(model_width))[None, :]
    return (own_rows, needle_score)


def solution(mesh):
    fsdp_size, tp_size = mesh.devices.shape
    split_mesh = Mesh(mesh.devices.reshape(fsdp_size, tp_size // 2, 2), ("fsdp",) + TP)
    in_specs = (
        P(("fsdp",) + TP, None),
        P(),
        P(None, "fsdp", TP),
        P(TP, None),
        P("fsdp", None),
        P("fsdp", None),
        P(),
    )
    out_specs = (P(("fsdp",) + TP, None), P("fsdp", None))
    return jax.shard_map(
        local, mesh=split_mesh, in_specs=in_specs, out_specs=out_specs, check_vma=False
    )
```

```python
import math

import jax
import jax.numpy as jnp
from jax import lax
from jax.experimental.layout import Layout, with_layout_constraint
from jax.sharding import PartitionSpec as P

EPSILON = 1e-06


def short_conv(gated_prod, tap_table, segments):
    length = gated_prod.shape[0]
    filtered = jnp.zeros(gated_prod.shape, jnp.float32)
    for offset in range(tap_table.shape[1]):
        shifted = jnp.pad(gated_prod, ((offset, 0), (0, 0)))[:length]
        earlier = jnp.pad(segments, (offset, 0), constant_values=-1)[:length]
        same_doc = (earlier == segments).astype(jnp.float32)
        filtered = filtered + shifted * same_doc[:, None] * tap_table[:, offset][None, :]
    return filtered


def gather_weights(proj_weight, fsdp_size, z_size):
    fsdp = lax.axis_index("fsdp")
    x_lo = fsdp // z_size
    x_swap = [(f, (f + z_size) % fsdp_size) for f in range(fsdp_size)]
    z_up = [(f, (f // z_size) * z_size + (f + 1) % z_size) for f in range(fsdp_size)]
    z_down = [(f, (f // z_size) * z_size + (f - 1) % z_size) for f in range(fsdp_size)]
    other = lax.ppermute(proj_weight, "fsdp", x_swap)
    first = jnp.where(x_lo == 0, proj_weight, other)
    second = jnp.where(x_lo == 0, other, proj_weight)
    pair = jnp.stack([first, second], axis=1)
    lead, halves, block, width = pair.shape
    buffer = with_layout_constraint(
        jnp.zeros((lead, halves, z_size, block, width), pair.dtype), Layout((0, 1, 2, 3, 4))
    )

    def place(into, arrived):
        for at, piece in arrived:
            into = lax.dynamic_update_slice(into, piece[:, :, None], (0, 0, at, 0, 0))
        return into

    arrivals = [[(0, pair)]]
    right = pair
    left = pair
    for step in range(1, z_size // 2):
        if step >= 2:
            buffer = place(buffer, arrivals[step - 2])
            right, left, buffer = lax.optimization_barrier((right, left, buffer))
        right = lax.ppermute(right, "fsdp", z_up)
        left = lax.ppermute(left, "fsdp", z_down)
        arrivals.append([(step, left), (z_size - step, right)])
    buffer = place(buffer, arrivals[-2])
    sent_a, sent_b, buffer = lax.optimization_barrier((right[:, :1], left[:, 1:], buffer))
    last_a = lax.ppermute(sent_a, "fsdp", z_up)
    last_b = lax.ppermute(sent_b, "fsdp", z_down)
    last = jnp.concatenate([last_a, last_b], axis=1)
    buffer = place(buffer, arrivals[-1] + [(z_size // 2, last)])
    buffer = with_layout_constraint(buffer, Layout((0, 1, 2, 3, 4)))
    return buffer.reshape(lead, fsdp_size * block, width)


def local(activations, norm_gain, proj_weight, short_filter, segment_ids, needle_pos, readout):
    model_width = activations.shape[1]
    local_rows = activations.shape[0]
    tp_size = lax.axis_size("tp")
    fsdp_size = lax.axis_size("fsdp")
    z_size = fsdp_size // 2
    channels = proj_weight.shape[2]
    block = proj_weight.shape[1]
    weights = gather_weights(proj_weight, fsdp_size, z_size)
    values = activations.astype(jnp.float32)
    scaled = lax.rsqrt(jnp.mean(values * values, axis=1, keepdims=True) + EPSILON)
    normed = (values * scaled * norm_gain[None, :]).astype(jnp.bfloat16)
    z = lax.axis_index("fsdp") % z_size
    grid = normed.reshape(local_rows, 2, z_size, block)
    doubled = jnp.concatenate([grid, grid], axis=2)
    rotated = lax.dynamic_slice_in_dim(doubled, z, z_size, axis=2).reshape(local_rows, model_width)
    spread = jnp.broadcast_to(rotated[None], (tp_size,) + rotated.shape)
    slab_rows = lax.all_to_all(spread, "tp", 0, 0, tiled=False).reshape(
        tp_size * local_rows, model_width
    )
    projected = jnp.einsum("sk,ikc->isc", slab_rows, weights, preferred_element_type=jnp.float32)
    projected = with_layout_constraint(projected, Layout((0, 1, 2)))
    gated_prod = projected[1] * projected[2]
    tap_table = jnp.repeat(short_filter, channels // short_filter.shape[0], axis=0)
    filtered = short_conv(gated_prod, tap_table, segment_ids[0])
    mixed_local = (projected[0] * filtered).astype(jnp.bfloat16)
    device_rank = lax.axis_index("tp")
    positions = needle_pos[0]
    slab_len = tp_size * local_rows
    picker = (positions[:, None] == jnp.arange(slab_len, dtype=jnp.int32)[None, :]).astype(
        jnp.bfloat16
    )
    picked = jnp.dot(picker, mixed_local, preferred_element_type=jnp.float32)
    own_readout = lax.dynamic_slice_in_dim(readout, device_rank * channels, channels, 0)
    partial_sum = jnp.sum(picked * own_readout[None, :], axis=1)
    rounded = lax.reduce_precision(partial_sum, exponent_bits=8, mantissa_bits=7)
    high = rounded.astype(jnp.bfloat16)
    low = (partial_sum - rounded).astype(jnp.bfloat16)
    extra_rows = 16
    extra = jnp.zeros((extra_rows, channels), jnp.bfloat16)
    extra = extra.at[0, : high.shape[0]].set(high).at[1, : low.shape[0]].set(low)
    blocks = mixed_local.reshape(tp_size, local_rows, channels)
    payload = jnp.concatenate(
        [blocks, jnp.broadcast_to(extra[None], (tp_size, extra_rows, channels))], axis=1
    )
    gathered = lax.all_to_all(payload, "tp", 0, 0, tiled=False)
    own_rows = jnp.transpose(gathered[:, :local_rows], (1, 0, 2)).reshape(
        local_rows, tp_size * channels
    )
    count = positions.shape[0]
    received = gathered[:, local_rows, :count].astype(jnp.float32) + gathered[
        :, local_rows + 1, :count
    ].astype(jnp.float32)
    needle_score = (jnp.sum(received, axis=0) / math.sqrt(model_width))[None, :]
    return (own_rows, needle_score)


def solution(mesh):
    in_specs = (
        P(("fsdp", "tp"), None),
        P(),
        P(None, "fsdp", "tp"),
        P("tp", None),
        P("fsdp", None),
        P("fsdp", None),
        P(),
    )
    out_specs = (P(("fsdp", "tp"), None), P("fsdp", None))
    return jax.shard_map(local, mesh=mesh, in_specs=in_specs, out_specs=out_specs, check_vma=False)
```

```python
import math

import jax
import jax.numpy as jnp
from jax import lax
from jax.experimental.layout import Layout, with_layout_constraint
from jax.sharding import PartitionSpec as P

EPSILON = 1e-06


def short_conv(gated_prod, tap_table, segments):
    length = gated_prod.shape[0]
    filtered = jnp.zeros(gated_prod.shape, jnp.float32)
    for offset in range(tap_table.shape[1]):
        shifted = jnp.pad(gated_prod, ((offset, 0), (0, 0)))[:length]
        earlier = jnp.pad(segments, (offset, 0), constant_values=-1)[:length]
        same_doc = (earlier == segments).astype(jnp.float32)
        filtered = filtered + shifted * same_doc[:, None] * tap_table[:, offset][None, :]
    return filtered


def gather_weights(proj_weight, fsdp_size, z_size):
    fsdp = lax.axis_index("fsdp")
    x_lo = fsdp // z_size
    x_swap = [(f, (f + z_size) % fsdp_size) for f in range(fsdp_size)]
    z_up = [(f, (f // z_size) * z_size + (f + 1) % z_size) for f in range(fsdp_size)]
    z_down = [(f, (f // z_size) * z_size + (f - 1) % z_size) for f in range(fsdp_size)]
    other = lax.ppermute(proj_weight, "fsdp", x_swap)
    first = jnp.where(x_lo == 0, proj_weight, other)
    second = jnp.where(x_lo == 0, other, proj_weight)
    pair = jnp.stack([first, second], axis=1)
    ahead = [pair]
    behind = []
    right = pair
    left = pair
    for _ in range(1, z_size // 2):
        right = lax.ppermute(right, "fsdp", z_up)
        left = lax.ppermute(left, "fsdp", z_down)
        behind.append(right)
        ahead.append(left)
    last_a = lax.ppermute(right[:, :1], "fsdp", z_up)
    last_b = lax.ppermute(left[:, 1:], "fsdp", z_down)
    ahead.append(jnp.concatenate([last_a, last_b], axis=1))
    pieces = ahead + behind[::-1]
    stacked = with_layout_constraint(jnp.stack(pieces, axis=2), Layout((0, 1, 2, 3, 4)))
    return stacked.reshape(
        proj_weight.shape[0], fsdp_size * proj_weight.shape[1], proj_weight.shape[2]
    )


def local(activations, norm_gain, proj_weight, short_filter, segment_ids, needle_pos, readout):
    model_width = activations.shape[1]
    local_rows = activations.shape[0]
    tp_size = lax.axis_size("tp")
    fsdp_size = lax.axis_size("fsdp")
    z_size = fsdp_size // 2
    channels = proj_weight.shape[2]
    block = proj_weight.shape[1]
    weights = gather_weights(proj_weight, fsdp_size, z_size)
    values = activations.astype(jnp.float32)
    scaled = lax.rsqrt(jnp.mean(values * values, axis=1, keepdims=True) + EPSILON)
    normed = (values * scaled * norm_gain[None, :]).astype(jnp.bfloat16)
    z = lax.axis_index("fsdp") % z_size
    grid = normed.reshape(local_rows, 2, z_size, block)
    doubled = jnp.concatenate([grid, grid], axis=2)
    rotated = lax.dynamic_slice_in_dim(doubled, z, z_size, axis=2).reshape(local_rows, model_width)
    spread = jnp.broadcast_to(rotated[None], (tp_size,) + rotated.shape)
    slab_rows = lax.all_to_all(spread, "tp", 0, 0, tiled=False).reshape(
        tp_size * local_rows, model_width
    )
    projected = jnp.einsum("sk,ikc->isc", slab_rows, weights, preferred_element_type=jnp.float32)
    projected = with_layout_constraint(projected, Layout((0, 1, 2)))
    gated_prod = projected[1] * projected[2]
    tap_table = jnp.repeat(short_filter, channels // short_filter.shape[0], axis=0)
    filtered = short_conv(gated_prod, tap_table, segment_ids[0])
    mixed_local = (projected[0] * filtered).astype(jnp.bfloat16)
    device_rank = lax.axis_index("tp")
    positions = needle_pos[0]
    slab_len = tp_size * local_rows
    picker = (positions[:, None] == jnp.arange(slab_len, dtype=jnp.int32)[None, :]).astype(
        jnp.bfloat16
    )
    picked = jnp.dot(picker, mixed_local, preferred_element_type=jnp.float32)
    own_readout = lax.dynamic_slice_in_dim(readout, device_rank * channels, channels, 0)
    partial_sum = jnp.sum(picked * own_readout[None, :], axis=1)
    rounded = lax.reduce_precision(partial_sum, exponent_bits=8, mantissa_bits=7)
    high = rounded.astype(jnp.bfloat16)
    low = (partial_sum - rounded).astype(jnp.bfloat16)
    lanes = 128
    extra_rows = 16
    extra = jnp.zeros((extra_rows, lanes), jnp.bfloat16)
    extra = extra.at[0, : high.shape[0]].set(high).at[1, : low.shape[0]].set(low)
    pieces = channels // lanes
    blocks = jnp.transpose(
        mixed_local.reshape(tp_size, local_rows, pieces, lanes), (0, 2, 1, 3)
    ).reshape(tp_size, pieces * local_rows, lanes)
    payload = jnp.concatenate(
        [blocks, jnp.broadcast_to(extra[None], (tp_size, extra_rows, lanes))], axis=1
    )
    gathered = lax.all_to_all(payload, "tp", 0, 0, tiled=False)
    own_rows = jnp.transpose(
        gathered[:, : pieces * local_rows].reshape(tp_size, pieces, local_rows, lanes), (2, 0, 1, 3)
    ).reshape(local_rows, tp_size * channels)
    data_rows = pieces * local_rows
    count = positions.shape[0]
    received = gathered[:, data_rows, :count].astype(jnp.float32) + gathered[
        :, data_rows + 1, :count
    ].astype(jnp.float32)
    needle_score = (jnp.sum(received, axis=0) / math.sqrt(model_width))[None, :]
    return (own_rows, needle_score)


def solution(mesh):
    in_specs = (
        P(("fsdp", "tp"), None),
        P(),
        P(None, "fsdp", "tp"),
        P("tp", None),
        P("fsdp", None),
        P("fsdp", None),
        P(),
    )
    out_specs = (P(("fsdp", "tp"), None), P("fsdp", None))
    return jax.shard_map(local, mesh=mesh, in_specs=in_specs, out_specs=out_specs, check_vma=False)
```

```python
import math

import jax
import jax.numpy as jnp
from jax import lax
from jax.experimental.layout import Layout, with_layout_constraint
from jax.sharding import PartitionSpec as P

EPSILON = 1e-06


def short_conv(gated_prod, tap_table, segments):
    length = gated_prod.shape[0]
    filtered = jnp.zeros(gated_prod.shape, jnp.float32)
    for offset in range(tap_table.shape[1]):
        shifted = jnp.pad(gated_prod, ((offset, 0), (0, 0)))[:length]
        earlier = jnp.pad(segments, (offset, 0), constant_values=-1)[:length]
        same_doc = (earlier == segments).astype(jnp.float32)
        filtered = filtered + shifted * same_doc[:, None] * tap_table[:, offset][None, :]
    return filtered


def gather_weights(proj_weight, fsdp_size, z_size):
    fsdp = lax.axis_index("fsdp")
    x_lo = fsdp // z_size
    x_swap = [(f, (f + z_size) % fsdp_size) for f in range(fsdp_size)]
    z_up = [(f, (f // z_size) * z_size + (f + 1) % z_size) for f in range(fsdp_size)]
    z_down = [(f, (f // z_size) * z_size + (f - 1) % z_size) for f in range(fsdp_size)]
    other = lax.ppermute(proj_weight, "fsdp", x_swap)
    first = jnp.where(x_lo == 0, proj_weight, other)
    second = jnp.where(x_lo == 0, other, proj_weight)
    pair = jnp.stack([first, second], axis=1)
    ahead = [pair]
    behind = []
    right = pair
    left = pair
    for _ in range(1, z_size // 2):
        right = lax.ppermute(right, "fsdp", z_up)
        left = lax.ppermute(left, "fsdp", z_down)
        behind.append(right)
        ahead.append(left)
    last_a = lax.ppermute(right[:, :1], "fsdp", z_up)
    last_b = lax.ppermute(left[:, 1:], "fsdp", z_down)
    ahead.append(jnp.concatenate([last_a, last_b], axis=1))
    pieces = ahead + behind[::-1]
    stacked = with_layout_constraint(jnp.stack(pieces, axis=2), Layout((0, 1, 2, 3, 4)))
    return stacked.reshape(
        proj_weight.shape[0], fsdp_size * proj_weight.shape[1], proj_weight.shape[2]
    )


def local(activations, norm_gain, proj_weight, short_filter, segment_ids, needle_pos, readout):
    model_width = activations.shape[1]
    local_rows = activations.shape[0]
    tp_size = lax.axis_size("tp")
    fsdp_size = lax.axis_size("fsdp")
    z_size = fsdp_size // 2
    channels = proj_weight.shape[2]
    block = proj_weight.shape[1]
    values = activations.astype(jnp.float32)
    scaled = lax.rsqrt(jnp.mean(values * values, axis=1, keepdims=True) + EPSILON)
    normed = (values * scaled * norm_gain[None, :]).astype(jnp.bfloat16)
    z = lax.axis_index("fsdp") % z_size
    grid = normed.reshape(local_rows, 2, z_size, block)
    doubled = jnp.concatenate([grid, grid], axis=2)
    rotated = lax.dynamic_slice_in_dim(doubled, z, z_size, axis=2).reshape(local_rows, model_width)
    spread = jnp.broadcast_to(rotated[None], (tp_size,) + rotated.shape)
    spread, own_weights = lax.optimization_barrier((spread, proj_weight))
    weights = gather_weights(own_weights, fsdp_size, z_size)
    slab_rows = lax.all_to_all(spread, "tp", 0, 0, tiled=False).reshape(
        tp_size * local_rows, model_width
    )
    projected = jnp.einsum("sk,ikc->isc", slab_rows, weights, preferred_element_type=jnp.float32)
    projected = with_layout_constraint(projected, Layout((0, 1, 2)))
    gated_prod = projected[1] * projected[2]
    tap_table = jnp.repeat(short_filter, channels // short_filter.shape[0], axis=0)
    filtered = short_conv(gated_prod, tap_table, segment_ids[0])
    mixed_local = (projected[0] * filtered).astype(jnp.bfloat16)
    device_rank = lax.axis_index("tp")
    positions = needle_pos[0]
    slab_len = tp_size * local_rows
    picker = (positions[:, None] == jnp.arange(slab_len, dtype=jnp.int32)[None, :]).astype(
        jnp.bfloat16
    )
    picked = jnp.dot(picker, mixed_local, preferred_element_type=jnp.float32)
    own_readout = lax.dynamic_slice_in_dim(readout, device_rank * channels, channels, 0)
    partial_sum = jnp.sum(picked * own_readout[None, :], axis=1)
    rounded = lax.reduce_precision(partial_sum, exponent_bits=8, mantissa_bits=7)
    high = rounded.astype(jnp.bfloat16)
    low = (partial_sum - rounded).astype(jnp.bfloat16)
    lanes = 128
    extra_rows = 16
    extra = jnp.zeros((extra_rows, lanes), jnp.bfloat16)
    extra = extra.at[0, : high.shape[0]].set(high).at[1, : low.shape[0]].set(low)
    pieces = channels // lanes
    blocks = jnp.transpose(
        mixed_local.reshape(tp_size, local_rows, pieces, lanes), (0, 2, 1, 3)
    ).reshape(tp_size, pieces * local_rows, lanes)
    payload = jnp.concatenate(
        [blocks, jnp.broadcast_to(extra[None], (tp_size, extra_rows, lanes))], axis=1
    )
    gathered = lax.all_to_all(payload, "tp", 0, 0, tiled=False)
    own_rows = jnp.transpose(
        gathered[:, : pieces * local_rows].reshape(tp_size, pieces, local_rows, lanes), (2, 0, 1, 3)
    ).reshape(local_rows, tp_size * channels)
    data_rows = pieces * local_rows
    count = positions.shape[0]
    received = gathered[:, data_rows, :count].astype(jnp.float32) + gathered[
        :, data_rows + 1, :count
    ].astype(jnp.float32)
    needle_score = (jnp.sum(received, axis=0) / math.sqrt(model_width))[None, :]
    return (own_rows, needle_score)


def solution(mesh):
    in_specs = (
        P(("fsdp", "tp"), None),
        P(),
        P(None, "fsdp", "tp"),
        P("tp", None),
        P("fsdp", None),
        P("fsdp", None),
        P(),
    )
    out_specs = (P(("fsdp", "tp"), None), P("fsdp", None))
    return jax.shard_map(local, mesh=mesh, in_specs=in_specs, out_specs=out_specs, check_vma=False)
```

```python
import math

import jax
import jax.numpy as jnp
from jax import lax
from jax.experimental.layout import Layout, with_layout_constraint
from jax.sharding import PartitionSpec as P

EPSILON = 1e-06


def short_conv(gated_prod, tap_table, segments):
    length = gated_prod.shape[0]
    filtered = jnp.zeros(gated_prod.shape, jnp.float32)
    for offset in range(tap_table.shape[1]):
        shifted = jnp.pad(gated_prod, ((offset, 0), (0, 0)))[:length]
        earlier = jnp.pad(segments, (offset, 0), constant_values=-1)[:length]
        same_doc = (earlier == segments).astype(jnp.float32)
        filtered = filtered + shifted * same_doc[:, None] * tap_table[:, offset][None, :]
    return filtered


def gather_weights(proj_weight, fsdp_size, z_size, companion):
    fsdp = lax.axis_index("fsdp")
    x_lo = fsdp // z_size
    x_swap = [(f, (f + z_size) % fsdp_size) for f in range(fsdp_size)]
    z_up = [(f, (f // z_size) * z_size + (f + 1) % z_size) for f in range(fsdp_size)]
    z_down = [(f, (f // z_size) * z_size + (f - 1) % z_size) for f in range(fsdp_size)]
    other = lax.ppermute(proj_weight, "fsdp", x_swap)
    first = jnp.where(x_lo == 0, proj_weight, other)
    second = jnp.where(x_lo == 0, other, proj_weight)
    pair = jnp.stack([first, second], axis=1)
    ahead = [pair]
    behind = []
    right = pair
    left = pair
    for _ in range(1, z_size // 2):
        right = lax.ppermute(right, "fsdp", z_up)
        left = lax.ppermute(left, "fsdp", z_down)
        behind.append(right)
        ahead.append(left)
    sent_a, sent_b, companion = lax.optimization_barrier((right[:, :1], left[:, 1:], companion))
    last_a = lax.ppermute(sent_a, "fsdp", z_up)
    last_b = lax.ppermute(sent_b, "fsdp", z_down)
    last = jnp.concatenate([last_a, last_b], axis=1)
    stacked = with_layout_constraint(
        jnp.stack(ahead + behind[::-1], axis=1), Layout((0, 1, 2, 3, 4))
    )
    lead, count, halves, block, width = stacked.shape
    early = stacked.reshape(lead, count * halves * block, width)
    return early, last.reshape(lead, halves * block, width), companion


def local(activations, norm_gain, proj_weight, short_filter, segment_ids, needle_pos, readout):
    model_width = activations.shape[1]
    local_rows = activations.shape[0]
    tp_size = lax.axis_size("tp")
    fsdp_size = lax.axis_size("fsdp")
    z_size = fsdp_size // 2
    channels = proj_weight.shape[2]
    block = proj_weight.shape[1]
    values = activations.astype(jnp.float32)
    scaled = lax.rsqrt(jnp.mean(values * values, axis=1, keepdims=True) + EPSILON)
    normed = (values * scaled * norm_gain[None, :]).astype(jnp.bfloat16)
    z = lax.axis_index("fsdp") % z_size
    half = z_size // 2
    grid = jnp.transpose(normed.reshape(local_rows, 2, z_size, block), (0, 2, 1, 3))
    doubled = jnp.concatenate([grid, grid], axis=1)
    ordered = jnp.concatenate(
        [
            lax.dynamic_slice_in_dim(doubled, z, half, axis=1),
            lax.dynamic_slice_in_dim(doubled, z + half + 1, half - 1, axis=1),
            lax.dynamic_slice_in_dim(doubled, z + half, 1, axis=1),
        ],
        axis=1,
    ).reshape(local_rows, model_width)
    spread = jnp.broadcast_to(ordered[None], (tp_size,) + ordered.shape)
    slab_rows = lax.all_to_all(spread, "tp", 0, 0, tiled=False).reshape(
        tp_size * local_rows, model_width
    )
    early_weights, last_weights, slab_rows = gather_weights(
        proj_weight, fsdp_size, z_size, slab_rows
    )
    split = early_weights.shape[1]
    early = jnp.einsum(
        "sk,ikc->isc", slab_rows[:, :split], early_weights, preferred_element_type=jnp.float32
    )
    early = lax.optimization_barrier(early)
    projected = early + jnp.einsum(
        "sk,ikc->isc", slab_rows[:, split:], last_weights, preferred_element_type=jnp.float32
    )
    projected = with_layout_constraint(projected, Layout((0, 1, 2)))
    gated_prod = projected[1] * projected[2]
    tap_table = jnp.repeat(short_filter, channels // short_filter.shape[0], axis=0)
    filtered = short_conv(gated_prod, tap_table, segment_ids[0])
    mixed_local = (projected[0] * filtered).astype(jnp.bfloat16)
    device_rank = lax.axis_index("tp")
    positions = needle_pos[0]
    slab_len = tp_size * local_rows
    picker = (positions[:, None] == jnp.arange(slab_len, dtype=jnp.int32)[None, :]).astype(
        jnp.bfloat16
    )
    picked = jnp.dot(picker, mixed_local, preferred_element_type=jnp.float32)
    own_readout = lax.dynamic_slice_in_dim(readout, device_rank * channels, channels, 0)
    partial_sum = jnp.sum(picked * own_readout[None, :], axis=1)
    rounded = lax.reduce_precision(partial_sum, exponent_bits=8, mantissa_bits=7)
    high = rounded.astype(jnp.bfloat16)
    low = (partial_sum - rounded).astype(jnp.bfloat16)
    lanes = 128
    extra_rows = 16
    extra = jnp.zeros((extra_rows, lanes), jnp.bfloat16)
    extra = extra.at[0, : high.shape[0]].set(high).at[1, : low.shape[0]].set(low)
    pieces = channels // lanes
    blocks = jnp.transpose(
        mixed_local.reshape(tp_size, local_rows, pieces, lanes), (0, 2, 1, 3)
    ).reshape(tp_size, pieces * local_rows, lanes)
    payload = jnp.concatenate(
        [blocks, jnp.broadcast_to(extra[None], (tp_size, extra_rows, lanes))], axis=1
    )
    gathered = lax.all_to_all(payload, "tp", 0, 0, tiled=False)
    own_rows = jnp.transpose(
        gathered[:, : pieces * local_rows].reshape(tp_size, pieces, local_rows, lanes), (2, 0, 1, 3)
    ).reshape(local_rows, tp_size * channels)
    data_rows = pieces * local_rows
    count = positions.shape[0]
    received = gathered[:, data_rows, :count].astype(jnp.float32) + gathered[
        :, data_rows + 1, :count
    ].astype(jnp.float32)
    needle_score = (jnp.sum(received, axis=0) / math.sqrt(model_width))[None, :]
    return (own_rows, needle_score)


def solution(mesh):
    in_specs = (
        P(("fsdp", "tp"), None),
        P(),
        P(None, "fsdp", "tp"),
        P("tp", None),
        P("fsdp", None),
        P("fsdp", None),
        P(),
    )
    out_specs = (P(("fsdp", "tp"), None), P("fsdp", None))
    return jax.shard_map(local, mesh=mesh, in_specs=in_specs, out_specs=out_specs, check_vma=False)
```

```python
import math

import jax
import jax.numpy as jnp
from jax import lax
from jax.experimental.layout import Layout, with_layout_constraint
from jax.sharding import PartitionSpec as P

EPSILON = 1e-06


def short_conv(gated_prod, tap_table, segments):
    length = gated_prod.shape[0]
    filtered = jnp.zeros(gated_prod.shape, jnp.float32)
    for offset in range(tap_table.shape[1]):
        shifted = jnp.pad(gated_prod, ((offset, 0), (0, 0)))[:length]
        earlier = jnp.pad(segments, (offset, 0), constant_values=-1)[:length]
        same_doc = (earlier == segments).astype(jnp.float32)
        filtered = filtered + shifted * same_doc[:, None] * tap_table[:, offset][None, :]
    return filtered


def gather_weights(proj_weight, fsdp_size, z_size, companion):
    fsdp = lax.axis_index("fsdp")
    x_lo = fsdp // z_size
    x_swap = [(f, (f + z_size) % fsdp_size) for f in range(fsdp_size)]
    z_up = [(f, (f // z_size) * z_size + (f + 1) % z_size) for f in range(fsdp_size)]
    z_down = [(f, (f // z_size) * z_size + (f - 1) % z_size) for f in range(fsdp_size)]
    other = lax.ppermute(proj_weight, "fsdp", x_swap)
    first = jnp.where(x_lo == 0, proj_weight, other)
    second = jnp.where(x_lo == 0, other, proj_weight)
    pair = jnp.stack([first, second], axis=1)
    ahead = [pair]
    behind = []
    right = pair
    left = pair
    last_ring_step = z_size // 2 - 1
    for step in range(1, last_ring_step + 1):
        if step == last_ring_step:
            right, left, companion = lax.optimization_barrier((right, left, companion))
        right = lax.ppermute(right, "fsdp", z_up)
        left = lax.ppermute(left, "fsdp", z_down)
        behind.append(right)
        ahead.append(left)
    last_a = lax.ppermute(right[:, :1], "fsdp", z_up)
    last_b = lax.ppermute(left[:, 1:], "fsdp", z_down)
    last = jnp.concatenate([last_a, last_b], axis=1)
    lead, halves, block, width = pair.shape
    kept = last_ring_step - 1
    groups = [ahead[: kept + 1] + behind[: kept][::-1], ahead[kept + 1 :] + behind[kept:]]
    stacks = []
    for group in groups:
        stacked = with_layout_constraint(jnp.stack(group, axis=1), Layout((0, 1, 2, 3, 4)))
        stacks.append(stacked.reshape(lead, len(group) * halves * block, width))
    return stacks, last.reshape(lead, halves * block, width), companion


def local(activations, norm_gain, proj_weight, short_filter, segment_ids, needle_pos, readout):
    model_width = activations.shape[1]
    local_rows = activations.shape[0]
    tp_size = lax.axis_size("tp")
    fsdp_size = lax.axis_size("fsdp")
    z_size = fsdp_size // 2
    channels = proj_weight.shape[2]
    block = proj_weight.shape[1]
    values = activations.astype(jnp.float32)
    scaled = lax.rsqrt(jnp.mean(values * values, axis=1, keepdims=True) + EPSILON)
    normed = (values * scaled * norm_gain[None, :]).astype(jnp.bfloat16)
    z = lax.axis_index("fsdp") % z_size
    grid = jnp.transpose(normed.reshape(local_rows, 2, z_size, block), (0, 2, 1, 3))
    doubled = jnp.concatenate([grid, grid], axis=1)
    runs = [(0, 7), (10, 6), (7, 1), (9, 1), (8, 1)]
    ordered = jnp.concatenate(
        [lax.dynamic_slice_in_dim(doubled, z + first, size, axis=1) for first, size in runs],
        axis=1,
    ).reshape(local_rows, model_width)
    spread = jnp.broadcast_to(ordered[None], (tp_size,) + ordered.shape)
    slab_rows = lax.all_to_all(spread, "tp", 0, 0, tiled=False).reshape(
        tp_size * local_rows, model_width
    )
    (first_weights, second_weights), last_weights, slab_rows = gather_weights(
        proj_weight, fsdp_size, z_size, slab_rows
    )
    cut = first_weights.shape[1]
    split = cut + second_weights.shape[1]
    early = lax.optimization_barrier(
        jnp.einsum("sk,ikc->isc", slab_rows[:, :cut], first_weights, preferred_element_type=jnp.float32)
    )
    early = lax.optimization_barrier(
        early
        + jnp.einsum(
            "sk,ikc->isc", slab_rows[:, cut:split], second_weights, preferred_element_type=jnp.float32
        )
    )
    projected = early + jnp.einsum(
        "sk,ikc->isc", slab_rows[:, split:], last_weights, preferred_element_type=jnp.float32
    )
    projected = with_layout_constraint(projected, Layout((0, 1, 2)))
    gated_prod = projected[1] * projected[2]
    tap_table = jnp.repeat(short_filter, channels // short_filter.shape[0], axis=0)
    filtered = short_conv(gated_prod, tap_table, segment_ids[0])
    mixed_local = (projected[0] * filtered).astype(jnp.bfloat16)
    device_rank = lax.axis_index("tp")
    positions = needle_pos[0]
    slab_len = tp_size * local_rows
    picker = (positions[:, None] == jnp.arange(slab_len, dtype=jnp.int32)[None, :]).astype(
        jnp.bfloat16
    )
    picked = jnp.dot(picker, mixed_local, preferred_element_type=jnp.float32)
    own_readout = lax.dynamic_slice_in_dim(readout, device_rank * channels, channels, 0)
    partial_sum = jnp.sum(picked * own_readout[None, :], axis=1)
    rounded = lax.reduce_precision(partial_sum, exponent_bits=8, mantissa_bits=7)
    high = rounded.astype(jnp.bfloat16)
    low = (partial_sum - rounded).astype(jnp.bfloat16)
    lanes = 128
    extra_rows = 16
    extra = jnp.zeros((extra_rows, lanes), jnp.bfloat16)
    extra = extra.at[0, : high.shape[0]].set(high).at[1, : low.shape[0]].set(low)
    pieces = channels // lanes
    blocks = jnp.transpose(
        mixed_local.reshape(tp_size, local_rows, pieces, lanes), (0, 2, 1, 3)
    ).reshape(tp_size, pieces * local_rows, lanes)
    payload = jnp.concatenate(
        [blocks, jnp.broadcast_to(extra[None], (tp_size, extra_rows, lanes))], axis=1
    )
    gathered = lax.all_to_all(payload, "tp", 0, 0, tiled=False)
    own_rows = jnp.transpose(
        gathered[:, : pieces * local_rows].reshape(tp_size, pieces, local_rows, lanes), (2, 0, 1, 3)
    ).reshape(local_rows, tp_size * channels)
    data_rows = pieces * local_rows
    count = positions.shape[0]
    received = gathered[:, data_rows, :count].astype(jnp.float32) + gathered[
        :, data_rows + 1, :count
    ].astype(jnp.float32)
    needle_score = (jnp.sum(received, axis=0) / math.sqrt(model_width))[None, :]
    return (own_rows, needle_score)


def solution(mesh):
    in_specs = (
        P(("fsdp", "tp"), None),
        P(),
        P(None, "fsdp", "tp"),
        P("tp", None),
        P("fsdp", None),
        P("fsdp", None),
        P(),
    )
    out_specs = (P(("fsdp", "tp"), None), P("fsdp", None))
    return jax.shard_map(local, mesh=mesh, in_specs=in_specs, out_specs=out_specs, check_vma=False)
```
